256 devices in a mesh: sky: 64 (over y, z, core), visit: 4 (over x).
Axes of the slice: x: 4, y: 4, z: 8, core: 2. Of those that a mesh axis runs over, the one named last changes fastest.
Arguments:
- science: float32 [32, 4096, 256], P('visit', 'sky'), may hold values from -6 to 6
- inv_variance: float32 [32, 4096, 256], P('visit', 'sky'), may hold values from 0.3 to 3
- psf_kernel: float32 [11, 11], replicated, may hold values from 0.01 to 0.12
- offsets: int32 [32, 16], replicated, may hold values from -2 to 2, as said below
Outputs:
- likelihood: float32 [16, 4096, 256], P(None, ('sky', 'visit'))
The draws below stay inside these ranges and needn't reach their ends.
Inputs may be any that keep to these rules, and one draw needn't show every extreme that they name: offsets[0, k] is 0 for every velocity; offsets[31, 0] is 2 and offsets[31, 1] is -2.
All inputs are finite; a program needn't handle non-finite values.
Results may differ from the reference program's by a relative error of at most 0.0001.
Values sent between devices are 32-bit elements; how exact they have to be, the bound alone decides.
No kernel may reach another device: no remote copies, remote signals or barrier semaphores. Data moves between devices by JAX's collectives and lax.ppermute only.
A program may use at most 64 MiB of HBM per device.

```python
import math
import jax
import jax.numpy as jnp
from jax import lax

V = 32
K = 16
PR = 5
BR = 8
MAXOFF = 2
W = 256
H = 4096


def draw_offsets(key, part):
    drawn = jax.random.randint(key, (V, K), -MAXOFF, MAXOFF + 1)
    drawn = drawn.at[0, :].set(0)
    drawn = drawn.at[V - 1, 0].set(MAXOFF)
    drawn = drawn.at[V - 1, 1].set(-MAXOFF)
    return drawn.astype(jnp.int32)


def steps_of(own_key, shape, shards, smallest, high):
    loudness, own = 1.0, jax.random.fold_in(own_key, 6)
    for dim, shards_of in shards:
        heights = jnp.exp(jax.random.uniform(jax.random.fold_in(own, dim), (shards_of,), jnp.float32, smallest / len(shards), high / len(shards)))
        loudness = loudness * jnp.repeat(heights, shape[dim] // shards_of).reshape([-1 if axis == dim else 1 for axis in range(len(shape))])
    return loudness


def bell_draw(stream_key, dims, width, limit, split=(), kind=jnp.bfloat16):
    values = width * jax.random.normal(stream_key, dims, jnp.float32)
    if split:
        values = values * steps_of(stream_key, dims, split, -0.22, 0.18)
    return jnp.clip(values, -limit, limit).astype(kind)


def setup_inputs(seed: int = 0) -> dict:
    streams_of = jax.random.split(jax.random.key(seed), 5)
    return {
        "science": bell_draw(streams_of[0], (V, H, W), 1.0, 6.0, ((0, 4), (1, 64)), jnp.float32),
        "inv_variance": jnp.clip(jnp.exp(math.log(3.0) - 2.3025851 * jax.random.uniform(streams_of[1], (V, H, W), jnp.float32) ** steps_of(streams_of[1], (V, H, W), ((0, 4), (1, 64)), -0.2, 0.2)), 0.3, 3.0),
        "psf_kernel": jnp.clip(jnp.exp(jax.random.uniform(streams_of[2], (2 * PR + 1, 2 * PR + 1), jnp.float32, math.log(0.01), math.log(0.12))), 0.01, 0.12),
        "offsets": draw_offsets(jax.random.fold_in(streams_of[4], 71), 0),
    }


def reference(science, inv_variance, psf_kernel, offsets):
    radius = (psf_kernel.shape[0] - 1) // 2
    kernel_size = 2 * radius + 1
    weights = jnp.stack([psf_kernel, psf_kernel * psf_kernel])

    def correlate_visit(visit_pair):
        sci_rows, inv_rows = visit_pair
        paired = jnp.stack([sci_rows * inv_rows, inv_rows])
        padded = jnp.pad(paired, ((0, 0), (radius, radius), (radius, radius)))
        running = jnp.zeros(paired.shape, jnp.float32)
        for row_tap in range(kernel_size):
            for col_tap in range(kernel_size):
                running = running + weights[:, row_tap, col_tap][:, None, None] * padded[:, row_tap:row_tap + H, col_tap:col_tap + W]
        return running
    images = lax.map(correlate_visit, (science, inv_variance))
    reach_rows = MAXOFF * BR
    padded = jnp.pad(images, ((0, 0), (0, 0), (reach_rows, reach_rows), (0, 0)))
    stacked = jnp.zeros((2, K, H, W), jnp.float32)
    for offset_value in range(-MAXOFF, MAXOFF + 1):
        onehot = (offsets == offset_value).astype(jnp.float32)
        start_row = reach_rows + offset_value * BR
        window = padded[:, :, start_row:start_row + H, :]
        stacked = stacked + jnp.einsum('tk,tcrw->ckrw', onehot, window, precision=lax.Precision.HIGHEST)
    return stacked[0] / jnp.sqrt(stacked[1])
```

```python
import jax
import jax.numpy as jnp
from jax import lax
from jax.sharding import PartitionSpec as P

BR = 8
MAXOFF = 2


def bordered_rows(block, axis, width):
    count = lax.axis_size(axis)
    forward = [(i, i + 1) for i in range(count - 1)]
    backward = [(target, source) for source, target in forward]
    dim = block.ndim - 2
    low = lax.ppermute(
        lax.slice_in_dim(block, block.shape[dim] - width, None, axis=dim), axis, forward
    )
    high = lax.ppermute(lax.slice_in_dim(block, 0, width, axis=dim), axis, backward)
    return jnp.concatenate([low, block, high], axis=dim)


def toeplitz(taps, cols):
    size = taps.shape[1]
    radius = (size - 1) // 2
    w = lax.broadcasted_iota(jnp.int32, (size, cols, cols), 1)
    v = lax.broadcasted_iota(jnp.int32, (size, cols, cols), 2)
    b = lax.broadcasted_iota(jnp.int32, (size, cols, cols), 0)
    onehot = (w - v + radius == b).astype(jnp.float32)
    return jnp.einsum("ab,bwv->awv", taps, onehot, precision=lax.Precision.HIGHEST)


def correlate_rows(bordered, kernel):
    return lax.conv_general_dilated(
        bordered,
        kernel,
        window_strides=(1,),
        padding="VALID",
        dimension_numbers=("NHC", "HIO", "NHC"),
        precision=lax.Precision.HIGH,
        preferred_element_type=jnp.float32,
    )


def shards(science, inv_variance, psf_kernel, offsets):
    radius = (psf_kernel.shape[0] - 1) // 2
    reach = MAXOFF * BR
    visits, rows, cols = science.shape
    total_rows = rows * lax.axis_size("sky")

    weighted = science * inv_variance
    both = jnp.stack([weighted, inv_variance])
    bordered = bordered_rows(both, "sky", radius + reach)

    psi = correlate_rows(bordered[0], toeplitz(psf_kernel, cols))
    phi = correlate_rows(bordered[1], toeplitz(psf_kernel * psf_kernel, cols))
    images = jnp.stack([psi, phi])

    first = lax.axis_index("sky") * rows - reach
    row_ids = first + lax.broadcasted_iota(jnp.int32, (1, 1, rows + 2 * reach, 1), 2)
    inside = (row_ids >= 0) & (row_ids < total_rows)
    images = jnp.where(inside, images, 0.0)

    mine = lax.dynamic_slice_in_dim(offsets, lax.axis_index("visit") * visits, visits, 0)
    partial = jnp.zeros((2, offsets.shape[1], rows, cols), jnp.float32)
    for offset_value in range(-MAXOFF, MAXOFF + 1):
        onehot = (mine == offset_value).astype(jnp.float32)
        start = reach + offset_value * BR
        window = images[:, :, start : start + rows, :]
        partial = partial + jnp.einsum(
            "tk,ctrw->ckrw", onehot, window, precision=lax.Precision.HIGHEST
        )

    stacked = lax.psum_scatter(partial, "visit", scatter_dimension=2, tiled=True)
    return stacked[0] / jnp.sqrt(stacked[1])


def solution(mesh):
    return jax.shard_map(
        shards,
        mesh=mesh,
        in_specs=(P("visit", "sky", None), P("visit", "sky", None), P(), P()),
        out_specs=P(None, ("sky", "visit"), None),
        check_vma=False,
    )
```

```python
import jax
import jax.numpy as jnp
from jax import lax
from jax.sharding import PartitionSpec as P

BR = 8
MAXOFF = 2


def bordered_rows(block, axis, width):
    count = lax.axis_size(axis)
    forward = [(i, i + 1) for i in range(count - 1)]
    backward = [(target, source) for source, target in forward]
    dim = block.ndim - 2
    low = lax.ppermute(
        lax.slice_in_dim(block, block.shape[dim] - width, None, axis=dim), axis, forward
    )
    high = lax.ppermute(lax.slice_in_dim(block, 0, width, axis=dim), axis, backward)
    return jnp.concatenate([low, block, high], axis=dim)


def toeplitz(taps, cols):
    size = taps.shape[1]
    radius = (size - 1) // 2
    w = lax.broadcasted_iota(jnp.int32, (size, cols, cols), 1)
    v = lax.broadcasted_iota(jnp.int32, (size, cols, cols), 2)
    b = lax.broadcasted_iota(jnp.int32, (size, cols, cols), 0)
    onehot = (w - v + radius == b).astype(jnp.float32)
    return jnp.einsum("ab,bwv->awv", taps, onehot, precision=lax.Precision.HIGHEST)


def correlate_rows(bordered, kernel):
    return lax.conv_general_dilated(
        bordered,
        kernel,
        window_strides=(1,),
        padding="VALID",
        dimension_numbers=("NHC", "HIO", "NHC"),
        precision=lax.Precision.HIGH,
        preferred_element_type=jnp.float32,
    )


def ring_reduce_scatter(partial, axis):
    count = lax.axis_size(axis)
    if count != 4:
        return lax.psum_scatter(partial, axis, scatter_dimension=2, tiled=True)
    me = lax.axis_index(axis)
    rows = partial.shape[2] // count
    half = partial.shape[3] // 2
    right = [(i, (i + 1) % count) for i in range(count)]
    left = [(i, (i - 1) % count) for i in range(count)]

    def block(step):
        return lax.dynamic_slice_in_dim(partial, ((me + step) % count) * rows, rows, axis=2)

    far = block(2)
    from_left = lax.ppermute(far[..., :half], axis, right)
    from_right = lax.ppermute(far[..., half:], axis, left)
    ahead = block(1)
    ahead = jnp.concatenate([ahead[..., :half] + from_left, ahead[..., half:]], axis=-1)
    behind = block(count - 1)
    behind = jnp.concatenate([behind[..., :half], behind[..., half:] + from_right], axis=-1)
    got_left = lax.ppermute(ahead, axis, right)
    got_right = lax.ppermute(behind, axis, left)
    return block(0) + got_left + got_right


def shards(science, inv_variance, psf_kernel, offsets):
    radius = (psf_kernel.shape[0] - 1) // 2
    reach = MAXOFF * BR
    visits, rows, cols = science.shape
    total_rows = rows * lax.axis_size("sky")

    weighted = science * inv_variance
    both = jnp.stack([weighted, inv_variance])
    bordered = bordered_rows(both, "sky", radius + reach)

    psi = correlate_rows(bordered[0], toeplitz(psf_kernel, cols))
    phi = correlate_rows(bordered[1], toeplitz(psf_kernel * psf_kernel, cols))
    images = jnp.stack([psi, phi])

    first = lax.axis_index("sky") * rows - reach
    row_ids = first + lax.broadcasted_iota(jnp.int32, (1, 1, rows + 2 * reach, 1), 2)
    inside = (row_ids >= 0) & (row_ids < total_rows)
    images = jnp.where(inside, images, 0.0)

    mine = lax.dynamic_slice_in_dim(offsets, lax.axis_index("visit") * visits, visits, 0)
    partial = jnp.zeros((2, offsets.shape[1], rows, cols), jnp.float32)
    for offset_value in range(-MAXOFF, MAXOFF + 1):
        onehot = (mine == offset_value).astype(jnp.float32)
        start = reach + offset_value * BR
        window = images[:, :, start : start + rows, :]
        partial = partial + jnp.einsum(
            "tk,ctrw->ckrw", onehot, window, precision=lax.Precision.HIGHEST
        )

    stacked = ring_reduce_scatter(partial, "visit")
    return stacked[0] / jnp.sqrt(stacked[1])


def solution(mesh):
    return jax.shard_map(
        shards,
        mesh=mesh,
        in_specs=(P("visit", "sky", None), P("visit", "sky", None), P(), P()),
        out_specs=P(None, ("sky", "visit"), None),
        check_vma=False,
    )
```

```python
import jax
import jax.numpy as jnp
from jax import lax
from jax.sharding import PartitionSpec as P

BR = 8
MAXOFF = 2


def bordered_rows(block, axis, width):
    count = lax.axis_size(axis)
    forward = [(i, i + 1) for i in range(count - 1)]
    backward = [(target, source) for source, target in forward]
    dim = block.ndim - 2
    low = lax.ppermute(
        lax.slice_in_dim(block, block.shape[dim] - width, None, axis=dim), axis, forward
    )
    high = lax.ppermute(lax.slice_in_dim(block, 0, width, axis=dim), axis, backward)
    return jnp.concatenate([low, block, high], axis=dim)


def toeplitz(taps, cols):
    size = taps.shape[1]
    shape = (size, cols + size - 1, cols)
    i = lax.broadcasted_iota(jnp.int32, shape, 1)
    o = lax.broadcasted_iota(jnp.int32, shape, 2)
    b = lax.broadcasted_iota(jnp.int32, shape, 0)
    onehot = (i - o == b).astype(jnp.float32)
    return jnp.einsum("ab,bio->aio", taps, onehot, precision=lax.Precision.HIGHEST)


def correlate_rows(bordered, kernel):
    return lax.conv_general_dilated(
        bordered,
        kernel,
        window_strides=(1,),
        padding="VALID",
        dimension_numbers=("NHC", "HIO", "NHC"),
        precision=lax.Precision.HIGH,
        preferred_element_type=jnp.float32,
    )


def ring_reduce_scatter(partial, axis):
    count = lax.axis_size(axis)
    if count != 4:
        return lax.psum_scatter(partial, axis, scatter_dimension=2, tiled=True)
    me = lax.axis_index(axis)
    rows = partial.shape[2] // count
    half = partial.shape[1] // 2
    right = [(i, (i + 1) % count) for i in range(count)]
    left = [(i, (i - 1) % count) for i in range(count)]

    def block(step):
        return lax.dynamic_slice_in_dim(partial, ((me + step) % count) * rows, rows, axis=2)

    far = block(2)
    from_left = lax.ppermute(far[:, :half], axis, right)
    from_right = lax.ppermute(far[:, half:], axis, left)
    ahead = block(1)
    ahead = jnp.concatenate([ahead[:, :half] + from_left, ahead[:, half:]], axis=1)
    behind = block(count - 1)
    behind = jnp.concatenate([behind[:, :half], behind[:, half:] + from_right], axis=1)
    got_left = lax.ppermute(ahead, axis, right)
    got_right = lax.ppermute(behind, axis, left)
    return block(0) + got_left + got_right


def shards(science, inv_variance, psf_kernel, offsets):
    radius = (psf_kernel.shape[0] - 1) // 2
    reach = MAXOFF * BR
    visits, rows, cols = science.shape
    total_rows = rows * lax.axis_size("sky")

    weighted = science * inv_variance
    both = jnp.stack([weighted, inv_variance])
    bordered = bordered_rows(both, "sky", radius + reach)

    chunk = 128 if cols % 128 == 0 else cols
    padded = jnp.pad(bordered, ((0, 0), (0, 0), (0, 0), (radius, radius)))
    kernels = [toeplitz(psf_kernel, chunk), toeplitz(psf_kernel * psf_kernel, chunk)]

    first = lax.axis_index("sky") * rows - reach
    row_ids = first + lax.broadcasted_iota(jnp.int32, (1, 1, rows + 2 * reach, 1), 2)
    inside = (row_ids >= 0) & (row_ids < total_rows)
    mine = lax.dynamic_slice_in_dim(offsets, lax.axis_index("visit") * visits, visits, 0)

    pieces = []
    for start_col in range(0, cols, chunk):
        window = padded[..., start_col : start_col + chunk + 2 * radius]
        images = jnp.stack([correlate_rows(window[c], kernels[c]) for c in range(2)])
        images = jnp.where(inside, images, 0.0)
        partial = jnp.zeros((2, offsets.shape[1], rows, chunk), jnp.float32)
        for offset_value in range(-MAXOFF, MAXOFF + 1):
            onehot = (mine == offset_value).astype(jnp.float32)
            start = reach + offset_value * BR
            shifted = images[:, :, start : start + rows, :]
            partial = partial + jnp.einsum(
                "tk,ctrw->ckrw", onehot, shifted, precision=lax.Precision.HIGHEST
            )
        stacked = ring_reduce_scatter(partial, "visit")
        pieces.append(stacked[0] / jnp.sqrt(stacked[1]))
    return jnp.concatenate(pieces, axis=-1)


def solution(mesh):
    return jax.shard_map(
        shards,
        mesh=mesh,
        in_specs=(P("visit", "sky", None), P("visit", "sky", None), P(), P()),
        out_specs=P(None, ("sky", "visit"), None),
        check_vma=False,
    )
```

```python
import jax
import jax.numpy as jnp
from jax import lax
from jax.sharding import PartitionSpec as P

BR = 8
MAXOFF = 2


def bordered_rows(block, axis, width):
    count = lax.axis_size(axis)
    forward = [(i, i + 1) for i in range(count - 1)]
    backward = [(target, source) for source, target in forward]
    dim = block.ndim - 2
    low = lax.ppermute(
        lax.slice_in_dim(block, block.shape[dim] - width, None, axis=dim), axis, forward
    )
    high = lax.ppermute(lax.slice_in_dim(block, 0, width, axis=dim), axis, backward)
    return jnp.concatenate([low, block, high], axis=dim)


def toeplitz(taps, cols):
    size = taps.shape[1]
    shape = (size, cols + size - 1, cols)
    i = lax.broadcasted_iota(jnp.int32, shape, 1)
    o = lax.broadcasted_iota(jnp.int32, shape, 2)
    b = lax.broadcasted_iota(jnp.int32, shape, 0)
    onehot = (i - o == b).astype(jnp.float32)
    return jnp.einsum("ab,bio->aio", taps, onehot, precision=lax.Precision.HIGHEST)


def correlate_rows(bordered, kernel):
    return lax.conv_general_dilated(
        bordered,
        kernel,
        window_strides=(1,),
        padding="VALID",
        dimension_numbers=("NHC", "HIO", "NHC"),
        precision=lax.Precision.HIGH,
        preferred_element_type=jnp.float32,
    )


def ring_step_one(partial, axis):
    me = lax.axis_index(axis)
    count = lax.axis_size(axis)
    rows = partial.shape[1] // count
    half = partial.shape[0] // 2
    blocks = [
        lax.dynamic_slice_in_dim(partial, ((me + step) % count) * rows, rows, axis=1)
        for step in range(count)
    ]
    right = [(i, (i + 1) % count) for i in range(count)]
    left = [(i, (i - 1) % count) for i in range(count)]
    from_left = lax.ppermute(blocks[2][:half], axis, right)
    from_right = lax.ppermute(blocks[2][half:], axis, left)
    return blocks, from_left, from_right


def ring_step_two(blocks, from_left, from_right, axis):
    count = lax.axis_size(axis)
    half = blocks[0].shape[0] // 2
    right = [(i, (i + 1) % count) for i in range(count)]
    left = [(i, (i - 1) % count) for i in range(count)]
    ahead = jnp.concatenate([blocks[1][:half] + from_left, blocks[1][half:]], axis=0)
    behind = jnp.concatenate([blocks[3][:half], blocks[3][half:] + from_right], axis=0)
    got_left = lax.ppermute(ahead, axis, right)
    got_right = lax.ppermute(behind, axis, left)
    return blocks[0] + got_left + got_right


def full_toeplitz(taps, cols, chunk):
    size = taps.shape[1]
    radius = (size - 1) // 2
    block = toeplitz(taps, chunk)
    parts = []
    for start_col in range(0, cols, chunk):
        low = start_col - radius
        first, last = max(0, -low), min(block.shape[1], cols - low)
        part = block[:, first:last, :]
        parts.append(jnp.pad(part, ((0, 0), (low + first, cols - (low + last)), (0, 0))))
    return jnp.concatenate(parts, axis=2)


def partial_sums(images, mine, rows):
    reach = MAXOFF * BR
    partial = jnp.zeros((mine.shape[1], rows, images.shape[2]), jnp.float32)
    for offset_value in range(-MAXOFF, MAXOFF + 1):
        onehot = (mine == offset_value).astype(jnp.float32)
        start = reach + offset_value * BR
        shifted = images[:, start : start + rows, :]
        partial = partial + jnp.einsum(
            "tk,trw->krw", onehot, shifted, precision=lax.Precision.HIGHEST
        )
    return partial


def shards(science, inv_variance, psf_kernel, offsets):
    radius = (psf_kernel.shape[0] - 1) // 2
    reach = MAXOFF * BR
    visits, rows, cols = science.shape
    total_rows = rows * lax.axis_size("sky")
    chunk = 128 if cols % 128 == 0 else cols

    first = lax.axis_index("sky") * rows - reach
    row_ids = first + lax.broadcasted_iota(jnp.int32, (1, rows + 2 * reach, 1), 1)
    inside = (row_ids >= 0) & (row_ids < total_rows)
    mine = lax.dynamic_slice_in_dim(offsets, lax.axis_index("visit") * visits, visits, 0)

    weighted = bordered_rows(science * inv_variance, "sky", radius + reach)
    inverse = bordered_rows(inv_variance, "sky", radius + reach)

    if lax.axis_size("visit") != 4:
        psi = correlate_rows(weighted, full_toeplitz(psf_kernel, cols, chunk))
        phi = correlate_rows(inverse, full_toeplitz(psf_kernel * psf_kernel, cols, chunk))
        both = jnp.stack([partial_sums(jnp.where(inside, x, 0.0), mine, rows) for x in (psi, phi)])
        both = lax.psum_scatter(both, "visit", scatter_dimension=2, tiled=True)
        return both[0] / jnp.sqrt(both[1])

    psi = correlate_rows(weighted, full_toeplitz(psf_kernel, cols, chunk))
    psi = partial_sums(jnp.where(inside, psi, 0.0), mine, rows)
    psi, inverse = lax.optimization_barrier((psi, inverse))
    blocks, from_left, from_right = ring_step_one(psi, "visit")

    phi = correlate_rows(inverse, full_toeplitz(psf_kernel * psf_kernel, cols, chunk))
    phi = jnp.where(inside, phi, 0.0)
    from_left, from_right, phi = lax.optimization_barrier((from_left, from_right, phi))
    psi = ring_step_two(blocks, from_left, from_right, "visit")

    phi = partial_sums(phi, mine, rows)
    phi = ring_step_two(*ring_step_one(phi, "visit"), "visit")
    return psi / jnp.sqrt(phi)


def solution(mesh):
    return jax.shard_map(
        shards,
        mesh=mesh,
        in_specs=(P("visit", "sky", None), P("visit", "sky", None), P(), P()),
        out_specs=P(None, ("sky", "visit"), None),
        check_vma=False,
    )
```

```python
import jax
import jax.numpy as jnp
from jax import lax
from jax.sharding import PartitionSpec as P
from jax.experimental import pallas as pl
from jax.experimental.pallas import tpu as pltpu

BR = 8
MAXOFF = 2


def bordered_rows(block, axis, width):
    count = lax.axis_size(axis)
    forward = [(i, i + 1) for i in range(count - 1)]
    backward = [(target, source) for source, target in forward]
    dim = block.ndim - 2
    low = lax.ppermute(
        lax.slice_in_dim(block, block.shape[dim] - width, None, axis=dim), axis, forward
    )
    high = lax.ppermute(lax.slice_in_dim(block, 0, width, axis=dim), axis, backward)
    return jnp.concatenate([low, block, high], axis=dim)


def toeplitz(taps, cols):
    size = taps.shape[1]
    radius = (size - 1) // 2
    w = lax.broadcasted_iota(jnp.int32, (size, cols, cols), 1)
    v = lax.broadcasted_iota(jnp.int32, (size, cols, cols), 2)
    b = lax.broadcasted_iota(jnp.int32, (size, cols, cols), 0)
    onehot = (w - v + radius == b).astype(jnp.float32)
    return jnp.einsum("ab,bwv->awv", taps, onehot, precision=lax.Precision.HIGHEST)


def correlate_rows(bordered, kernel):
    return lax.conv_general_dilated(
        bordered,
        kernel,
        window_strides=(1,),
        padding="VALID",
        dimension_numbers=("NHC", "HIO", "NHC"),
        precision=lax.Precision.HIGH,
        preferred_element_type=jnp.float32,
    )


def ring_reduce_scatter(partial, axis):
    count = lax.axis_size(axis)
    if count != 4:
        return lax.psum_scatter(partial, axis, scatter_dimension=2, tiled=True)
    me = lax.axis_index(axis)
    rows = partial.shape[2] // count
    half = partial.shape[3] // 2
    right = [(i, (i + 1) % count) for i in range(count)]
    left = [(i, (i - 1) % count) for i in range(count)]

    def block(step):
        return lax.dynamic_slice_in_dim(partial, ((me + step) % count) * rows, rows, axis=2)

    far = block(2)
    from_left = lax.ppermute(far[..., :half], axis, right)
    from_right = lax.ppermute(far[..., half:], axis, left)
    ahead = block(1)
    ahead = jnp.concatenate([ahead[..., :half] + from_left, ahead[..., half:]], axis=-1)
    behind = block(count - 1)
    behind = jnp.concatenate([behind[..., :half], behind[..., half:] + from_right], axis=-1)
    got_left = lax.ppermute(ahead, axis, right)
    got_right = lax.ppermute(behind, axis, left)
    return block(0) + got_left + got_right


def stack_kernel(offsets_ref, images_ref, out_ref):
    visits = images_ref.shape[1]
    rows = out_ref.shape[2]
    reach = MAXOFF * BR
    for k in range(out_ref.shape[1]):
        total = None
        for t in range(visits):
            start = pl.multiple_of(reach + BR * offsets_ref[t, k], BR)
            term = images_ref[0, t, pl.ds(start, rows), :]
            total = term if total is None else total + term
        out_ref[0, k] = total


def partial_sums(images, mine):
    channels, visits, extended, cols = images.shape
    rows = extended - 2 * MAXOFF * BR
    velocities = mine.shape[1]
    return pl.pallas_call(
        stack_kernel,
        out_shape=jax.ShapeDtypeStruct((channels, velocities, rows, cols), jnp.float32),
        grid_spec=pltpu.PrefetchScalarGridSpec(
            num_scalar_prefetch=1,
            grid=(channels,),
            in_specs=[pl.BlockSpec((1, visits, extended, cols), lambda c, off: (c, 0, 0, 0))],
            out_specs=pl.BlockSpec((1, velocities, rows, cols), lambda c, off: (c, 0, 0, 0)),
        ),
        cost_estimate=pl.CostEstimate(
            flops=channels * velocities * visits * rows * cols,
            transcendentals=0,
            bytes_accessed=4 * channels * (visits * extended + velocities * rows) * cols,
        ),
    )(mine, images)


def shards(science, inv_variance, psf_kernel, offsets):
    radius = (psf_kernel.shape[0] - 1) // 2
    reach = MAXOFF * BR
    visits, rows, cols = science.shape
    total_rows = rows * lax.axis_size("sky")

    weighted = science * inv_variance
    both = jnp.stack([weighted, inv_variance])
    bordered = bordered_rows(both, "sky", radius + reach)

    psi = correlate_rows(bordered[0], toeplitz(psf_kernel, cols))
    phi = correlate_rows(bordered[1], toeplitz(psf_kernel * psf_kernel, cols))
    images = jnp.stack([psi, phi])

    first = lax.axis_index("sky") * rows - reach
    row_ids = first + lax.broadcasted_iota(jnp.int32, (1, 1, rows + 2 * reach, 1), 2)
    inside = (row_ids >= 0) & (row_ids < total_rows)
    images = jnp.where(inside, images, 0.0)

    mine = lax.dynamic_slice_in_dim(offsets, lax.axis_index("visit") * visits, visits, 0)
    partial = partial_sums(images, mine)

    stacked = ring_reduce_scatter(partial, "visit")
    return stacked[0] / jnp.sqrt(stacked[1])


def solution(mesh):
    return jax.shard_map(
        shards,
        mesh=mesh,
        in_specs=(P("visit", "sky", None), P("visit", "sky", None), P(), P()),
        out_specs=P(None, ("sky", "visit"), None),
        check_vma=False,
    )
```

```python
import jax
import jax.numpy as jnp
from jax import lax
from jax.sharding import PartitionSpec as P
from jax.experimental import pallas as pl
from jax.experimental.pallas import tpu as pltpu

BR = 8
MAXOFF = 2


def bordered_rows(block, axis, width):
    count = lax.axis_size(axis)
    forward = [(i, i + 1) for i in range(count - 1)]
    backward = [(target, source) for source, target in forward]
    dim = block.ndim - 2
    low = lax.ppermute(
        lax.slice_in_dim(block, block.shape[dim] - width, None, axis=dim), axis, forward
    )
    high = lax.ppermute(lax.slice_in_dim(block, 0, width, axis=dim), axis, backward)
    return jnp.concatenate([low, block, high], axis=dim)


def toeplitz(taps, cols):
    size = taps.shape[1]
    radius = (size - 1) // 2
    w = lax.broadcasted_iota(jnp.int32, (size, cols, cols), 1)
    v = lax.broadcasted_iota(jnp.int32, (size, cols, cols), 2)
    b = lax.broadcasted_iota(jnp.int32, (size, cols, cols), 0)
    onehot = (w - v + radius == b).astype(jnp.float32)
    return jnp.einsum("ab,bwv->awv", taps, onehot, precision=lax.Precision.HIGHEST)


def correlate_rows(bordered, kernel):
    return lax.conv_general_dilated(
        bordered,
        kernel,
        window_strides=(1,),
        padding="VALID",
        dimension_numbers=("NHC", "HIO", "NHC"),
        precision=lax.Precision.HIGH,
        preferred_element_type=jnp.float32,
    )


def ring_reduce_scatter(partial, axis):
    count = lax.axis_size(axis)
    if count != 4:
        return lax.psum_scatter(partial, axis, scatter_dimension=2, tiled=True)
    me = lax.axis_index(axis)
    rows = partial.shape[2] // count
    half = partial.shape[3] // 2
    right = [(i, (i + 1) % count) for i in range(count)]
    left = [(i, (i - 1) % count) for i in range(count)]

    def block(step):
        return lax.dynamic_slice_in_dim(partial, ((me + step) % count) * rows, rows, axis=2)

    far = block(2)
    from_left = lax.ppermute(far[..., :half], axis, right)
    from_right = lax.ppermute(far[..., half:], axis, left)
    ahead = block(1)
    ahead = jnp.concatenate([ahead[..., :half] + from_left, ahead[..., half:]], axis=-1)
    behind = block(count - 1)
    behind = jnp.concatenate([behind[..., :half], behind[..., half:] + from_right], axis=-1)
    got_left = lax.ppermute(ahead, axis, right)
    got_right = lax.ppermute(behind, axis, left)
    return block(0) + got_left + got_right


def stack_kernel(offsets_ref, keep_ref, images_ref, out_ref, held_ref):
    visits, extended, _ = held_ref.shape
    rows = out_ref.shape[1]
    reach = MAXOFF * BR
    low = images_ref[:, 0:reach, :]
    high = images_ref[:, extended - reach :, :]
    held_ref[:, 0:reach, :] = jnp.where(keep_ref[0] > 0, low, 0.0)
    held_ref[:, reach : extended - reach, :] = images_ref[:, reach : extended - reach, :]
    held_ref[:, extended - reach :, :] = jnp.where(keep_ref[1] > 0, high, 0.0)
    for k in range(out_ref.shape[0]):
        total = None
        for t in range(visits):
            start = pl.multiple_of(reach + BR * offsets_ref[t, k], BR)
            term = held_ref[t, pl.ds(start, rows), :]
            total = term if total is None else total + term
        out_ref[k] = total


def partial_sums(images, mine, keep):
    visits, extended, cols = images.shape
    rows = extended - 2 * MAXOFF * BR
    velocities = mine.shape[1]
    return pl.pallas_call(
        stack_kernel,
        out_shape=jax.ShapeDtypeStruct((velocities, rows, cols), jnp.float32),
        grid_spec=pltpu.PrefetchScalarGridSpec(
            num_scalar_prefetch=2,
            grid=(1,),
            in_specs=[pl.BlockSpec((visits, extended, cols), lambda i, off, keep: (0, 0, 0))],
            out_specs=pl.BlockSpec((velocities, rows, cols), lambda i, off, keep: (0, 0, 0)),
            scratch_shapes=[pltpu.VMEM((visits, extended, cols), jnp.float32)],
        ),
        cost_estimate=pl.CostEstimate(
            flops=velocities * visits * rows * cols,
            transcendentals=0,
            bytes_accessed=4 * (visits * extended + velocities * rows) * cols,
        ),
    )(mine, keep, images)


def shards(science, inv_variance, psf_kernel, offsets):
    radius = (psf_kernel.shape[0] - 1) // 2
    reach = MAXOFF * BR
    visits, rows, cols = science.shape

    weighted = science * inv_variance
    both = jnp.stack([weighted, inv_variance])
    bordered = bordered_rows(both, "sky", radius + reach)

    psi = correlate_rows(bordered[0], toeplitz(psf_kernel, cols))
    phi = correlate_rows(bordered[1], toeplitz(psf_kernel * psf_kernel, cols))

    sky = lax.axis_index("sky")
    keep = jnp.stack([sky > 0, sky < lax.axis_size("sky") - 1]).astype(jnp.int32)
    mine = lax.dynamic_slice_in_dim(offsets, lax.axis_index("visit") * visits, visits, 0)
    partial = jnp.stack([partial_sums(psi, mine, keep), partial_sums(phi, mine, keep)])

    stacked = ring_reduce_scatter(partial, "visit")
    return stacked[0] / jnp.sqrt(stacked[1])


def solution(mesh):
    return jax.shard_map(
        shards,
        mesh=mesh,
        in_specs=(P("visit", "sky", None), P("visit", "sky", None), P(), P()),
        out_specs=P(None, ("sky", "visit"), None),
        check_vma=False,
    )
```

```python
import jax
import jax.numpy as jnp
from jax import lax
from jax.sharding import PartitionSpec as P

BR = 8
MAXOFF = 2


def bordered_rows(block, axis, width):
    count = lax.axis_size(axis)
    forward = [(i, i + 1) for i in range(count - 1)]
    backward = [(target, source) for source, target in forward]
    dim = block.ndim - 2
    low = lax.ppermute(
        lax.slice_in_dim(block, block.shape[dim] - width, None, axis=dim), axis, forward
    )
    high = lax.ppermute(lax.slice_in_dim(block, 0, width, axis=dim), axis, backward)
    return jnp.concatenate([low, block, high], axis=dim)


def toeplitz(taps, cols):
    size = taps.shape[1]
    shape = (size, cols + size - 1, cols)
    i = lax.broadcasted_iota(jnp.int32, shape, 1)
    o = lax.broadcasted_iota(jnp.int32, shape, 2)
    b = lax.broadcasted_iota(jnp.int32, shape, 0)
    onehot = (i - o == b).astype(jnp.float32)
    return jnp.einsum("ab,bio->aio", taps, onehot, precision=lax.Precision.HIGHEST)


def correlate_rows(bordered, kernel):
    return lax.conv_general_dilated(
        bordered,
        kernel,
        window_strides=(1,),
        padding="VALID",
        dimension_numbers=("NHC", "HIO", "NHC"),
        precision=lax.Precision.HIGH,
        preferred_element_type=jnp.float32,
    )


def ring_step_one(partial, axis):
    me = lax.axis_index(axis)
    count = lax.axis_size(axis)
    rows = partial.shape[1] // count
    half = partial.shape[0] // 2
    blocks = [
        lax.dynamic_slice_in_dim(partial, ((me + step) % count) * rows, rows, axis=1)
        for step in range(count)
    ]
    right = [(i, (i + 1) % count) for i in range(count)]
    left = [(i, (i - 1) % count) for i in range(count)]
    from_left = lax.ppermute(blocks[2][:half], axis, right)
    from_right = lax.ppermute(blocks[2][half:], axis, left)
    return blocks, from_left, from_right


def ring_step_two(blocks, from_left, from_right, axis):
    count = lax.axis_size(axis)
    half = blocks[0].shape[0] // 2
    right = [(i, (i + 1) % count) for i in range(count)]
    left = [(i, (i - 1) % count) for i in range(count)]
    ahead = jnp.concatenate([blocks[1][:half] + from_left, blocks[1][half:]], axis=0)
    behind = jnp.concatenate([blocks[3][:half], blocks[3][half:] + from_right], axis=0)
    got_left = lax.ppermute(ahead, axis, right)
    got_right = lax.ppermute(behind, axis, left)
    return blocks[0] + got_left + got_right


def toeplitz_full(taps, cols):
    size = taps.shape[1]
    radius = (size - 1) // 2
    w = lax.broadcasted_iota(jnp.int32, (size, cols, cols), 1)
    v = lax.broadcasted_iota(jnp.int32, (size, cols, cols), 2)
    b = lax.broadcasted_iota(jnp.int32, (size, cols, cols), 0)
    onehot = (w - v + radius == b).astype(jnp.float32)
    return jnp.einsum("ab,bwv->awv", taps, onehot, precision=lax.Precision.HIGHEST)


def partial_sums(images, mine, rows):
    reach = MAXOFF * BR
    partial = jnp.zeros((mine.shape[1], rows, images.shape[2]), jnp.float32)
    for offset_value in range(-MAXOFF, MAXOFF + 1):
        onehot = (mine == offset_value).astype(jnp.float32)
        start = reach + offset_value * BR
        shifted = images[:, start : start + rows, :]
        partial = partial + jnp.einsum(
            "tk,trw->krw", onehot, shifted, precision=lax.Precision.HIGHEST
        )
    return partial


def shards(science, inv_variance, psf_kernel, offsets):
    radius = (psf_kernel.shape[0] - 1) // 2
    reach = MAXOFF * BR
    visits, rows, cols = science.shape
    total_rows = rows * lax.axis_size("sky")

    first = lax.axis_index("sky") * rows - reach
    row_ids = first + lax.broadcasted_iota(jnp.int32, (1, rows + 2 * reach, 1), 1)
    inside = (row_ids >= 0) & (row_ids < total_rows)
    mine = lax.dynamic_slice_in_dim(offsets, lax.axis_index("visit") * visits, visits, 0)

    bordered = bordered_rows(jnp.stack([science * inv_variance, inv_variance]), "sky", radius + reach)
    weighted, inverse = bordered[0], bordered[1]

    if lax.axis_size("visit") != 4:
        psi = correlate_rows(weighted, toeplitz_full(psf_kernel, cols))
        phi = correlate_rows(inverse, toeplitz_full(psf_kernel * psf_kernel, cols))
        both = jnp.stack([partial_sums(jnp.where(inside, x, 0.0), mine, rows) for x in (psi, phi)])
        both = lax.psum_scatter(both, "visit", scatter_dimension=2, tiled=True)
        return both[0] / jnp.sqrt(both[1])

    psi = correlate_rows(weighted, toeplitz_full(psf_kernel, cols))
    psi = partial_sums(jnp.where(inside, psi, 0.0), mine, rows)
    psi, inverse = lax.optimization_barrier((psi, inverse))
    blocks, from_left, from_right = ring_step_one(psi, "visit")

    phi = correlate_rows(inverse, toeplitz_full(psf_kernel * psf_kernel, cols))
    phi = jnp.where(inside, phi, 0.0)
    from_left, from_right, phi = lax.optimization_barrier((from_left, from_right, phi))
    psi = ring_step_two(blocks, from_left, from_right, "visit")

    phi = partial_sums(phi, mine, rows)
    phi = ring_step_two(*ring_step_one(phi, "visit"), "visit")
    return psi / jnp.sqrt(phi)


def solution(mesh):
    return jax.shard_map(
        shards,
        mesh=mesh,
        in_specs=(P("visit", "sky", None), P("visit", "sky", None), P(), P()),
        out_specs=P(None, ("sky", "visit"), None),
        check_vma=False,
    )
```

```python
import jax
import jax.numpy as jnp
from jax import lax
from jax.sharding import PartitionSpec as P

BR = 8
MAXOFF = 2


def bordered_rows(block, axis, width):
    count = lax.axis_size(axis)
    forward = [(i, i + 1) for i in range(count - 1)]
    backward = [(target, source) for source, target in forward]
    dim = block.ndim - 2
    low = lax.ppermute(
        lax.slice_in_dim(block, block.shape[dim] - width, None, axis=dim), axis, forward
    )
    high = lax.ppermute(lax.slice_in_dim(block, 0, width, axis=dim), axis, backward)
    return jnp.concatenate([low, block, high], axis=dim)


def toeplitz(taps, cols):
    size = taps.shape[1]
    radius = (size - 1) // 2
    w = lax.broadcasted_iota(jnp.int32, (size, cols, cols), 1)
    v = lax.broadcasted_iota(jnp.int32, (size, cols, cols), 2)
    b = lax.broadcasted_iota(jnp.int32, (size, cols, cols), 0)
    onehot = (w - v + radius == b).astype(jnp.float32)
    return jnp.einsum("ab,bwv->awv", taps, onehot, precision=lax.Precision.HIGHEST)


def correlate_rows(bordered, kernel):
    return lax.conv_general_dilated(
        bordered,
        kernel,
        window_strides=(1,),
        padding="VALID",
        dimension_numbers=("NHC", "HIO", "NHC"),
        precision=lax.Precision.HIGH,
        preferred_element_type=jnp.float32,
    )


def ring_reduce_scatter(partial, axis):
    count = lax.axis_size(axis)
    if count != 4:
        return lax.psum_scatter(partial, axis, scatter_dimension=2, tiled=True)
    me = lax.axis_index(axis)
    rows = partial.shape[2] // count
    half = partial.shape[3] // 2
    right = [(i, (i + 1) % count) for i in range(count)]
    left = [(i, (i - 1) % count) for i in range(count)]

    def block(step):
        return lax.dynamic_slice_in_dim(partial, ((me + step) % count) * rows, rows, axis=2)

    far = block(2)
    from_left = lax.ppermute(far[..., :half], axis, right)
    from_right = lax.ppermute(far[..., half:], axis, left)
    ahead = block(1)
    ahead = jnp.concatenate([ahead[..., :half] + from_left, ahead[..., half:]], axis=-1)
    behind = block(count - 1)
    behind = jnp.concatenate([behind[..., :half], behind[..., half:] + from_right], axis=-1)
    got_left = lax.ppermute(ahead, axis, right)
    got_right = lax.ppermute(behind, axis, left)
    return block(0) + got_left + got_right


def shards(science, inv_variance, psf_kernel, offsets):
    radius = (psf_kernel.shape[0] - 1) // 2
    reach = MAXOFF * BR
    visits, rows, cols = science.shape
    total_rows = rows * lax.axis_size("sky")

    weighted = science * inv_variance
    both = jnp.stack([weighted, inv_variance])
    bordered = bordered_rows(both, "sky", radius + reach)

    taps = toeplitz(jnp.concatenate([psf_kernel, psf_kernel * psf_kernel]), cols)
    size = psf_kernel.shape[0]
    psi = correlate_rows(bordered[0], taps[:size])
    phi = correlate_rows(bordered[1], taps[size:])
    images = jnp.stack([psi, phi])

    first = lax.axis_index("sky") * rows - reach
    row_ids = first + lax.broadcasted_iota(jnp.int32, (1, 1, rows + 2 * reach, 1), 2)
    inside = (row_ids >= 0) & (row_ids < total_rows)
    images = jnp.where(inside, images, 0.0)

    mine = lax.dynamic_slice_in_dim(offsets, lax.axis_index("visit") * visits, visits, 0)
    partial = jnp.zeros((2, offsets.shape[1], rows, cols), jnp.float32)
    for offset_value in range(-MAXOFF, MAXOFF + 1):
        onehot = (mine == offset_value).astype(jnp.float32)
        start = reach + offset_value * BR
        window = images[:, :, start : start + rows, :]
        partial = partial + jnp.einsum(
            "tk,ctrw->ckrw", onehot, window, precision=lax.Precision.HIGH
        )

    stacked = ring_reduce_scatter(partial, "visit")
    return stacked[0] / jnp.sqrt(stacked[1])


def solution(mesh):
    return jax.shard_map(
        shards,
        mesh=mesh,
        in_specs=(P("visit", "sky", None), P("visit", "sky", None), P(), P()),
        out_specs=P(None, ("sky", "visit"), None),
        check_vma=False,
    )
```

```python
import jax
import jax.numpy as jnp
from jax import lax
from jax.sharding import PartitionSpec as P

BR = 8
MAXOFF = 2


def bordered_rows(block, axis, width):
    count = lax.axis_size(axis)
    forward = [(i, i + 1) for i in range(count - 1)]
    backward = [(target, source) for source, target in forward]
    dim = block.ndim - 2
    low = lax.ppermute(
        lax.slice_in_dim(block, block.shape[dim] - width, None, axis=dim), axis, forward
    )
    high = lax.ppermute(lax.slice_in_dim(block, 0, width, axis=dim), axis, backward)
    return jnp.concatenate([low, block, high], axis=dim)


def toeplitz(taps, cols):
    size = taps.shape[1]
    radius = (size - 1) // 2
    w = lax.broadcasted_iota(jnp.int32, (size, cols, cols), 1)
    v = lax.broadcasted_iota(jnp.int32, (size, cols, cols), 2)
    b = lax.broadcasted_iota(jnp.int32, (size, cols, cols), 0)
    onehot = (w - v + radius == b).astype(jnp.float32)
    return jnp.einsum("ab,bwv->awv", taps, onehot, precision=lax.Precision.HIGHEST)


def correlate_rows(bordered, kernel):
    return lax.conv_general_dilated(
        bordered,
        kernel,
        window_strides=(1,),
        padding="VALID",
        dimension_numbers=("NHC", "HIO", "NHC"),
        precision=lax.Precision.HIGH,
        preferred_element_type=jnp.float32,
    )


def split_permute(value, axis, pairs):
    half = value.shape[1] // 2
    return jnp.concatenate(
        [lax.ppermute(value[:, :half], axis, pairs), lax.ppermute(value[:, half:], axis, pairs)],
        axis=1,
    )


def ring_reduce_scatter(partial, axis):
    count = lax.axis_size(axis)
    if count != 4:
        return lax.psum_scatter(partial, axis, scatter_dimension=2, tiled=True)
    me = lax.axis_index(axis)
    rows = partial.shape[2] // count
    half = partial.shape[3] // 2
    right = [(i, (i + 1) % count) for i in range(count)]
    left = [(i, (i - 1) % count) for i in range(count)]

    def block(step):
        return lax.dynamic_slice_in_dim(partial, ((me + step) % count) * rows, rows, axis=2)

    far = block(2)
    from_left = split_permute(far[..., :half], axis, right)
    from_right = split_permute(far[..., half:], axis, left)
    ahead = block(1)
    ahead = jnp.concatenate([ahead[..., :half] + from_left, ahead[..., half:]], axis=-1)
    behind = block(count - 1)
    behind = jnp.concatenate([behind[..., :half], behind[..., half:] + from_right], axis=-1)
    got_left = split_permute(ahead, axis, right)
    got_right = split_permute(behind, axis, left)
    return block(0) + got_left + got_right


def shards(science, inv_variance, psf_kernel, offsets):
    radius = (psf_kernel.shape[0] - 1) // 2
    reach = MAXOFF * BR
    visits, rows, cols = science.shape
    total_rows = rows * lax.axis_size("sky")

    weighted = science * inv_variance
    both = jnp.stack([weighted, inv_variance])
    bordered = bordered_rows(both, "sky", radius + reach)

    psi = correlate_rows(bordered[0], toeplitz(psf_kernel, cols))
    phi = correlate_rows(bordered[1], toeplitz(psf_kernel * psf_kernel, cols))
    images = jnp.stack([psi, phi])

    first = lax.axis_index("sky") * rows - reach
    row_ids = first + lax.broadcasted_iota(jnp.int32, (1, 1, rows + 2 * reach, 1), 2)
    inside = (row_ids >= 0) & (row_ids < total_rows)
    images = jnp.where(inside, images, 0.0)

    mine = lax.dynamic_slice_in_dim(offsets, lax.axis_index("visit") * visits, visits, 0)
    partial = jnp.zeros((2, offsets.shape[1], rows, cols), jnp.float32)
    for offset_value in range(-MAXOFF, MAXOFF + 1):
        onehot = (mine == offset_value).astype(jnp.float32)
        start = reach + offset_value * BR
        window = images[:, :, start : start + rows, :]
        partial = partial + jnp.einsum(
            "tk,ctrw->ckrw", onehot, window, precision=lax.Precision.HIGHEST
        )

    stacked = ring_reduce_scatter(partial, "visit")
    return stacked[0] / jnp.sqrt(stacked[1])


def solution(mesh):
    return jax.shard_map(
        shards,
        mesh=mesh,
        in_specs=(P("visit", "sky", None), P("visit", "sky", None), P(), P()),
        out_specs=P(None, ("sky", "visit"), None),
        check_vma=False,
    )
```

```python
import jax
import jax.numpy as jnp
from jax import lax
from jax.sharding import PartitionSpec as P

BR = 8
MAXOFF = 2


def bordered_rows(block, axis, width):
    count = lax.axis_size(axis)
    forward = [(i, i + 1) for i in range(count - 1)]
    backward = [(target, source) for source, target in forward]
    dim = block.ndim - 2
    low = lax.ppermute(
        lax.slice_in_dim(block, block.shape[dim] - width, None, axis=dim), axis, forward
    )
    high = lax.ppermute(lax.slice_in_dim(block, 0, width, axis=dim), axis, backward)
    return jnp.concatenate([low, block, high], axis=dim)


def toeplitz(taps, cols):
    size = taps.shape[1]
    radius = (size - 1) // 2
    w = lax.broadcasted_iota(jnp.int32, (size, cols, cols), 1)
    v = lax.broadcasted_iota(jnp.int32, (size, cols, cols), 2)
    b = lax.broadcasted_iota(jnp.int32, (size, cols, cols), 0)
    onehot = (w - v + radius == b).astype(jnp.float32)
    return jnp.einsum("ab,bwv->awv", taps, onehot, precision=lax.Precision.HIGHEST)


def correlate_rows(bordered, kernel):
    return lax.conv_general_dilated(
        bordered,
        kernel,
        window_strides=(1,),
        padding="VALID",
        dimension_numbers=("NHC", "HIO", "NHC"),
        precision=lax.Precision.HIGH,
        preferred_element_type=jnp.float32,
    )


def ring_reduce_scatter(partial, axis):
    count = lax.axis_size(axis)
    if count != 4:
        return lax.psum_scatter(partial, axis, scatter_dimension=2, tiled=True)
    me = lax.axis_index(axis)
    rows = partial.shape[2] // count
    half = partial.shape[3] // 2
    right = [(i, (i + 1) % count) for i in range(count)]
    left = [(i, (i - 1) % count) for i in range(count)]

    def block(step):
        return lax.dynamic_slice_in_dim(partial, ((me + step) % count) * rows, rows, axis=2)

    far = block(2)
    from_left = lax.ppermute(far[..., :half], axis, right)
    from_right = lax.ppermute(far[..., half:], axis, left)
    ahead = block(1)
    ahead = jnp.concatenate([ahead[..., :half] + from_left, ahead[..., half:]], axis=-1)
    behind = block(count - 1)
    behind = jnp.concatenate([behind[..., :half], behind[..., half:] + from_right], axis=-1)
    got_left = lax.ppermute(ahead, axis, right)
    got_right = lax.ppermute(behind, axis, left)
    return block(0) + got_left + got_right


def shards(science, inv_variance, psf_kernel, offsets):
    radius = (psf_kernel.shape[0] - 1) // 2
    reach = MAXOFF * BR
    visits, rows, cols = science.shape
    total_rows = rows * lax.axis_size("sky")

    weighted = science * inv_variance
    both = jnp.stack([weighted, inv_variance])
    bordered = bordered_rows(both, "sky", radius + reach)

    psi = correlate_rows(bordered[0], toeplitz(psf_kernel, cols))
    phi = correlate_rows(bordered[1], toeplitz(psf_kernel * psf_kernel, cols))
    images = jnp.stack([psi, phi])

    first = lax.axis_index("sky") * rows - reach
    row_ids = first + lax.broadcasted_iota(jnp.int32, (1, 1, rows + 2 * reach, 1), 2)
    inside = (row_ids >= 0) & (row_ids < total_rows)
    images = jnp.where(inside, images, 0.0)

    mine = lax.dynamic_slice_in_dim(offsets, lax.axis_index("visit") * visits, visits, 0)
    shifts = range(-MAXOFF, MAXOFF + 1)
    onehot = jnp.stack([(mine == value).astype(jnp.float32) for value in shifts])
    windows = jnp.stack(
        [images[:, :, reach + value * BR : reach + value * BR + rows, :] for value in shifts], axis=1
    )
    partial = jnp.einsum(
        "otk,cotrw->ckrw", onehot, windows, precision=lax.Precision.HIGHEST
    )

    stacked = ring_reduce_scatter(partial, "visit")
    return stacked[0] / jnp.sqrt(stacked[1])


def solution(mesh):
    return jax.shard_map(
        shards,
        mesh=mesh,
        in_specs=(P("visit", "sky", None), P("visit", "sky", None), P(), P()),
        out_specs=P(None, ("sky", "visit"), None),
        check_vma=False,
    )
```

```python
import jax
import jax.numpy as jnp
from jax import lax
from jax.sharding import PartitionSpec as P

BR = 8
MAXOFF = 2


def bordered_rows(block, axis, width):
    count = lax.axis_size(axis)
    forward = [(i, i + 1) for i in range(count - 1)]
    backward = [(target, source) for source, target in forward]
    dim = block.ndim - 2
    low = lax.ppermute(
        lax.slice_in_dim(block, block.shape[dim] - width, None, axis=dim), axis, forward
    )
    high = lax.ppermute(lax.slice_in_dim(block, 0, width, axis=dim), axis, backward)
    return jnp.concatenate([low, block, high], axis=dim)


def toeplitz(taps, cols):
    size = taps.shape[1]
    radius = (size - 1) // 2
    w = lax.broadcasted_iota(jnp.int32, (size, cols, cols), 1)
    v = lax.broadcasted_iota(jnp.int32, (size, cols, cols), 2)
    b = lax.broadcasted_iota(jnp.int32, (size, cols, cols), 0)
    onehot = (w - v + radius == b).astype(jnp.float32)
    return jnp.einsum("ab,bwv->awv", taps, onehot, precision=lax.Precision.HIGHEST)


def correlate_rows(bordered, kernel):
    return lax.conv_general_dilated(
        bordered,
        kernel,
        window_strides=(1,),
        padding="VALID",
        dimension_numbers=("NHC", "HIO", "NHC"),
        precision=lax.Precision.HIGH,
        preferred_element_type=jnp.float32,
    )


def ring_reduce_scatter(partial, axis):
    count = lax.axis_size(axis)
    if count != 4:
        return lax.psum_scatter(partial, axis, scatter_dimension=2, tiled=True)
    me = lax.axis_index(axis)
    rows = partial.shape[2] // count
    half = partial.shape[3] // 2
    right = [(i, (i + 1) % count) for i in range(count)]
    left = [(i, (i - 1) % count) for i in range(count)]

    def block(step):
        return lax.dynamic_slice_in_dim(partial, ((me + step) % count) * rows, rows, axis=2)

    far, ahead, behind = block(2), block(1), block(count - 1)
    from_left = lax.ppermute(far[..., :half], axis, right)
    own_high = lax.ppermute(ahead[..., half:], axis, right)
    from_right = lax.ppermute(far[..., half:], axis, left)
    own_low = lax.ppermute(behind[..., :half], axis, left)
    got_low = lax.ppermute(ahead[..., :half] + from_left, axis, right)
    got_high = lax.ppermute(behind[..., half:] + from_right, axis, left)
    return block(0) + jnp.concatenate([got_low + own_low, got_high + own_high], axis=-1)


def shards(science, inv_variance, psf_kernel, offsets):
    radius = (psf_kernel.shape[0] - 1) // 2
    reach = MAXOFF * BR
    visits, rows, cols = science.shape
    total_rows = rows * lax.axis_size("sky")

    weighted = science * inv_variance
    both = jnp.stack([weighted, inv_variance])
    bordered = bordered_rows(both, "sky", radius + reach)

    psi = correlate_rows(bordered[0], toeplitz(psf_kernel, cols))
    phi = correlate_rows(bordered[1], toeplitz(psf_kernel * psf_kernel, cols))
    images = jnp.stack([psi, phi])

    first = lax.axis_index("sky") * rows - reach
    row_ids = first + lax.broadcasted_iota(jnp.int32, (1, 1, rows + 2 * reach, 1), 2)
    inside = (row_ids >= 0) & (row_ids < total_rows)
    images = jnp.where(inside, images, 0.0)

    mine = lax.dynamic_slice_in_dim(offsets, lax.axis_index("visit") * visits, visits, 0)
    shifts = range(-MAXOFF, MAXOFF + 1)
    onehot = jnp.stack([(mine == value).astype(jnp.float32) for value in shifts])
    windows = jnp.stack(
        [images[:, :, reach + value * BR : reach + value * BR + rows, :] for value in shifts], axis=1
    )
    partial = jnp.einsum(
        "otk,cotrw->ckrw", onehot, windows, precision=lax.Precision.HIGHEST
    )

    stacked = ring_reduce_scatter(partial, "visit")
    return stacked[0] / jnp.sqrt(stacked[1])


def solution(mesh):
    return jax.shard_map(
        shards,
        mesh=mesh,
        in_specs=(P("visit", "sky", None), P("visit", "sky", None), P(), P()),
        out_specs=P(None, ("sky", "visit"), None),
        check_vma=False,
    )
```

```python
import jax
import jax.numpy as jnp
from jax import lax
from jax.sharding import PartitionSpec as P

BR = 8
MAXOFF = 2


def bordered_rows(block, axis, width):
    count = lax.axis_size(axis)
    forward = [(i, i + 1) for i in range(count - 1)]
    backward = [(target, source) for source, target in forward]
    dim = block.ndim - 2
    low = lax.ppermute(
        lax.slice_in_dim(block, block.shape[dim] - width, None, axis=dim), axis, forward
    )
    high = lax.ppermute(lax.slice_in_dim(block, 0, width, axis=dim), axis, backward)
    return jnp.concatenate([low, block, high], axis=dim)


def toeplitz(taps, cols):
    size = taps.shape[1]
    radius = (size - 1) // 2
    w = lax.broadcasted_iota(jnp.int32, (1, cols, cols), 1)
    v = lax.broadcasted_iota(jnp.int32, (1, cols, cols), 2)
    tap = w - v + radius
    out = jnp.zeros((taps.shape[0], cols, cols), jnp.float32)
    for b in range(size):
        out = jnp.where(tap == b, taps[:, b][:, None, None], out)
    return out


def correlate_rows(bordered, kernel):
    return lax.conv_general_dilated(
        bordered,
        kernel,
        window_strides=(1,),
        padding="VALID",
        dimension_numbers=("NHC", "HIO", "NHC"),
        precision=lax.Precision.HIGH,
        preferred_element_type=jnp.float32,
    )


def ring_reduce_scatter(partial, axis):
    count = lax.axis_size(axis)
    if count != 4:
        return lax.psum_scatter(partial, axis, scatter_dimension=2, tiled=True)
    me = lax.axis_index(axis)
    rows = partial.shape[2] // count
    half = partial.shape[3] // 2
    right = [(i, (i + 1) % count) for i in range(count)]
    left = [(i, (i - 1) % count) for i in range(count)]

    def block(step):
        return lax.dynamic_slice_in_dim(partial, ((me + step) % count) * rows, rows, axis=2)

    far = block(2)
    from_left = lax.ppermute(far[..., :half], axis, right)
    from_right = lax.ppermute(far[..., half:], axis, left)
    ahead = block(1)
    ahead = jnp.concatenate([ahead[..., :half] + from_left, ahead[..., half:]], axis=-1)
    behind = block(count - 1)
    behind = jnp.concatenate([behind[..., :half], behind[..., half:] + from_right], axis=-1)
    got_left = lax.ppermute(ahead, axis, right)
    got_right = lax.ppermute(behind, axis, left)
    return block(0) + got_left + got_right


def shards(science, inv_variance, psf_kernel, offsets):
    radius = (psf_kernel.shape[0] - 1) // 2
    reach = MAXOFF * BR
    visits, rows, cols = science.shape
    total_rows = rows * lax.axis_size("sky")

    weighted = science * inv_variance
    both = jnp.stack([weighted, inv_variance])
    bordered = bordered_rows(both, "sky", radius + reach)

    psi = correlate_rows(bordered[0], toeplitz(psf_kernel, cols))
    phi = correlate_rows(bordered[1], toeplitz(psf_kernel * psf_kernel, cols))
    images = jnp.stack([psi, phi])

    first = lax.axis_index("sky") * rows - reach
    row_ids = first + lax.broadcasted_iota(jnp.int32, (1, 1, rows + 2 * reach, 1), 2)
    inside = (row_ids >= 0) & (row_ids < total_rows)
    images = jnp.where(inside, images, 0.0)

    mine = lax.dynamic_slice_in_dim(offsets, lax.axis_index("visit") * visits, visits, 0)
    shifts = range(-MAXOFF, MAXOFF + 1)
    onehot = jnp.stack([(mine == value).astype(jnp.float32) for value in shifts])
    windows = jnp.stack(
        [images[:, :, reach + value * BR : reach + value * BR + rows, :] for value in shifts], axis=1
    )
    partial = jnp.einsum(
        "otk,cotrw->ckrw", onehot, windows, precision=lax.Precision.HIGHEST
    )

    stacked = ring_reduce_scatter(partial, "visit")
    return stacked[0] / jnp.sqrt(stacked[1])


def solution(mesh):
    return jax.shard_map(
        shards,
        mesh=mesh,
        in_specs=(P("visit", "sky", None), P("visit", "sky", None), P(), P()),
        out_specs=P(None, ("sky", "visit"), None),
        check_vma=False,
    )
```

```python
import jax
import jax.numpy as jnp
from jax import lax
from jax.sharding import PartitionSpec as P

BR = 8
MAXOFF = 2


def bordered_rows(block, axis, width):
    count = lax.axis_size(axis)
    forward = [(i, i + 1) for i in range(count - 1)]
    backward = [(target, source) for source, target in forward]
    dim = block.ndim - 2
    low = lax.ppermute(
        lax.slice_in_dim(block, block.shape[dim] - width, None, axis=dim), axis, forward
    )
    high = lax.ppermute(lax.slice_in_dim(block, 0, width, axis=dim), axis, backward)
    return jnp.concatenate([low, block, high], axis=dim)


def toeplitz(taps, cols):
    size = taps.shape[1]
    radius = (size - 1) // 2
    w = lax.broadcasted_iota(jnp.int32, (1, cols, cols), 1)
    v = lax.broadcasted_iota(jnp.int32, (1, cols, cols), 2)
    tap = w - v + radius
    out = jnp.zeros((taps.shape[0], cols, cols), jnp.float32)
    for b in range(size):
        out = jnp.where(tap == b, taps[:, b][:, None, None], out)
    return out


def correlate_rows(bordered, kernel):
    return lax.conv_general_dilated(
        bordered,
        kernel,
        window_strides=(1,),
        padding="VALID",
        dimension_numbers=("NHC", "HIO", "NHC"),
        precision=lax.Precision.HIGH,
        preferred_element_type=jnp.float32,
    )


def ring_reduce_scatter(partial, axis):
    count = lax.axis_size(axis)
    if count != 4:
        return lax.psum_scatter(partial, axis, scatter_dimension=2, tiled=True)
    me = lax.axis_index(axis)
    rows = partial.shape[2] // count
    half = partial.shape[3] // 2
    right = [(i, (i + 1) % count) for i in range(count)]
    left = [(i, (i - 1) % count) for i in range(count)]

    def block(step):
        return lax.dynamic_slice_in_dim(partial, ((me + step) % count) * rows, rows, axis=2)

    far = block(2)
    from_left = lax.ppermute(far[..., :half], axis, right)
    from_right = lax.ppermute(far[..., half:], axis, left)
    ahead = block(1)
    ahead = jnp.concatenate([ahead[..., :half] + from_left, ahead[..., half:]], axis=-1)
    behind = block(count - 1)
    behind = jnp.concatenate([behind[..., :half], behind[..., half:] + from_right], axis=-1)
    got_left = lax.ppermute(ahead, axis, right)
    got_right = lax.ppermute(behind, axis, left)
    return block(0) + got_left + got_right


def shards(science, inv_variance, psf_kernel, offsets):
    radius = (psf_kernel.shape[0] - 1) // 2
    reach = MAXOFF * BR
    visits, rows, cols = science.shape
    total_rows = rows * lax.axis_size("sky")

    width = radius + reach
    count = lax.axis_size("sky")
    forward = [(i, i + 1) for i in range(count - 1)]
    backward = [(target, source) for source, target in forward]
    low = lax.ppermute(jnp.stack([science[:, rows - width :], inv_variance[:, rows - width :]]), "sky", forward)
    high = lax.ppermute(jnp.stack([science[:, :width], inv_variance[:, :width]]), "sky", backward)
    bordered = [
        jnp.concatenate([low[0] * low[1], science * inv_variance, high[0] * high[1]], axis=1),
        jnp.concatenate([low[1], inv_variance, high[1]], axis=1),
    ]

    psi = correlate_rows(bordered[0], toeplitz(psf_kernel, cols))
    phi = correlate_rows(bordered[1], toeplitz(psf_kernel * psf_kernel, cols))
    images = jnp.stack([psi, phi])

    first = lax.axis_index("sky") * rows - reach
    row_ids = first + lax.broadcasted_iota(jnp.int32, (1, 1, rows + 2 * reach, 1), 2)
    inside = (row_ids >= 0) & (row_ids < total_rows)
    images = jnp.where(inside, images, 0.0)

    mine = lax.dynamic_slice_in_dim(offsets, lax.axis_index("visit") * visits, visits, 0)
    shifts = range(-MAXOFF, MAXOFF + 1)
    onehot = jnp.stack([(mine == value).astype(jnp.float32) for value in shifts])
    windows = jnp.stack(
        [images[:, :, reach + value * BR : reach + value * BR + rows, :] for value in shifts], axis=1
    )
    partial = jnp.einsum(
        "otk,cotrw->ckrw", onehot, windows, precision=lax.Precision.HIGHEST
    )

    stacked = ring_reduce_scatter(partial, "visit")
    return stacked[0] / jnp.sqrt(stacked[1])


def solution(mesh):
    return jax.shard_map(
        shards,
        mesh=mesh,
        in_specs=(P("visit", "sky", None), P("visit", "sky", None), P(), P()),
        out_specs=P(None, ("sky", "visit"), None),
        check_vma=False,
    )
```

```python
import jax
import jax.numpy as jnp
from jax import lax
from jax.sharding import PartitionSpec as P

BR = 8
MAXOFF = 2


def bordered_rows(block, axis, width):
    count = lax.axis_size(axis)
    forward = [(i, i + 1) for i in range(count - 1)]
    backward = [(target, source) for source, target in forward]
    dim = block.ndim - 2
    low = lax.ppermute(
        lax.slice_in_dim(block, block.shape[dim] - width, None, axis=dim), axis, forward
    )
    high = lax.ppermute(lax.slice_in_dim(block, 0, width, axis=dim), axis, backward)
    return jnp.concatenate([low, block, high], axis=dim)


def toeplitz(taps, cols):
    size = taps.shape[1]
    radius = (size - 1) // 2
    w = lax.broadcasted_iota(jnp.int32, (1, cols, cols), 1)
    v = lax.broadcasted_iota(jnp.int32, (1, cols, cols), 2)
    tap = w - v + radius
    out = jnp.zeros((taps.shape[0], cols, cols), jnp.float32)
    for b in range(size):
        out = jnp.where(tap == b, taps[:, b][:, None, None], out)
    return out


def correlate_rows(bordered, kernel):
    return lax.conv_general_dilated(
        bordered,
        kernel,
        window_strides=(1,),
        padding="VALID",
        dimension_numbers=("NHC", "HIO", "NHC"),
        precision=lax.Precision.HIGH,
        preferred_element_type=jnp.float32,
    )


def ring_reduce_scatter(partial, axis):
    count = lax.axis_size(axis)
    if count != 4:
        return lax.psum_scatter(partial, axis, scatter_dimension=2, tiled=True)
    me = lax.axis_index(axis)
    rows = partial.shape[2] // count
    half = partial.shape[3] // 2
    right = [(i, (i + 1) % count) for i in range(count)]
    left = [(i, (i - 1) % count) for i in range(count)]

    def block(step):
        return lax.dynamic_slice_in_dim(partial, ((me + step) % count) * rows, rows, axis=2)

    far = block(2)
    from_left = lax.ppermute(far[..., :half], axis, right)
    from_right = lax.ppermute(far[..., half:], axis, left)
    ahead = block(1)
    ahead = jnp.concatenate([ahead[..., :half] + from_left, ahead[..., half:]], axis=-1)
    behind = block(count - 1)
    behind = jnp.concatenate([behind[..., :half], behind[..., half:] + from_right], axis=-1)
    got_left = lax.ppermute(ahead, axis, right)
    got_right = lax.ppermute(behind, axis, left)
    return block(0) + got_left + got_right


def shards(science, inv_variance, psf_kernel, offsets):
    radius = (psf_kernel.shape[0] - 1) // 2
    reach = MAXOFF * BR
    visits, rows, cols = science.shape
    total_rows = rows * lax.axis_size("sky")

    width = radius + reach
    count = lax.axis_size("sky")
    forward = [(i, i + 1) for i in range(count - 1)]
    backward = [(target, source) for source, target in forward]
    low = lax.ppermute(jnp.stack([science[:, rows - width :], inv_variance[:, rows - width :]]), "sky", forward)
    high = lax.ppermute(jnp.stack([science[:, :width], inv_variance[:, :width]]), "sky", backward)
    own = [science * inv_variance, inv_variance]
    lows = [low[0] * low[1], low[1]]
    highs = [high[0] * high[1], high[1]]
    reach_in = 2 * radius

    def correlated(c, kernel):
        interior = correlate_rows(own[c], kernel)
        top = correlate_rows(jnp.concatenate([lows[c], own[c][:, :reach_in]], axis=1), kernel)
        bottom = correlate_rows(jnp.concatenate([own[c][:, rows - reach_in :], highs[c]], axis=1), kernel)
        return jnp.concatenate([top, interior, bottom], axis=1)

    psi = correlated(0, toeplitz(psf_kernel, cols))
    phi = correlated(1, toeplitz(psf_kernel * psf_kernel, cols))
    images = jnp.stack([psi, phi])

    first = lax.axis_index("sky") * rows - reach
    row_ids = first + lax.broadcasted_iota(jnp.int32, (1, 1, rows + 2 * reach, 1), 2)
    inside = (row_ids >= 0) & (row_ids < total_rows)
    images = jnp.where(inside, images, 0.0)

    mine = lax.dynamic_slice_in_dim(offsets, lax.axis_index("visit") * visits, visits, 0)
    shifts = range(-MAXOFF, MAXOFF + 1)
    onehot = jnp.stack([(mine == value).astype(jnp.float32) for value in shifts])
    windows = jnp.stack(
        [images[:, :, reach + value * BR : reach + value * BR + rows, :] for value in shifts], axis=1
    )
    partial = jnp.einsum(
        "otk,cotrw->ckrw", onehot, windows, precision=lax.Precision.HIGHEST
    )

    stacked = ring_reduce_scatter(partial, "visit")
    return stacked[0] / jnp.sqrt(stacked[1])


def solution(mesh):
    return jax.shard_map(
        shards,
        mesh=mesh,
        in_specs=(P("visit", "sky", None), P("visit", "sky", None), P(), P()),
        out_specs=P(None, ("sky", "visit"), None),
        check_vma=False,
    )
```

```python
import jax
import jax.numpy as jnp
from jax import lax
from jax.sharding import PartitionSpec as P

BR = 8
MAXOFF = 2


def bordered_rows(block, axis, width):
    count = lax.axis_size(axis)
    forward = [(i, i + 1) for i in range(count - 1)]
    backward = [(target, source) for source, target in forward]
    dim = block.ndim - 2
    low = lax.ppermute(
        lax.slice_in_dim(block, block.shape[dim] - width, None, axis=dim), axis, forward
    )
    high = lax.ppermute(lax.slice_in_dim(block, 0, width, axis=dim), axis, backward)
    return jnp.concatenate([low, block, high], axis=dim)


def toeplitz(taps, cols):
    size = taps.shape[1]
    radius = (size - 1) // 2
    w = lax.broadcasted_iota(jnp.int32, (1, cols, cols), 1)
    v = lax.broadcasted_iota(jnp.int32, (1, cols, cols), 2)
    tap = w - v + radius
    out = jnp.zeros((taps.shape[0], cols, cols), jnp.float32)
    for b in range(size):
        out = jnp.where(tap == b, taps[:, b][:, None, None], out)
    return out


def correlate_rows(bordered, kernel):
    return lax.conv_general_dilated(
        bordered,
        kernel,
        window_strides=(1,),
        padding="VALID",
        dimension_numbers=("NHC", "HIO", "NHC"),
        precision=lax.Precision.HIGH,
        preferred_element_type=jnp.float32,
    )


def ring_reduce_scatter(partial, axis):
    count = lax.axis_size(axis)
    if count != 4:
        return lax.psum_scatter(partial, axis, scatter_dimension=2, tiled=True)
    me = lax.axis_index(axis)
    rows = partial.shape[2] // count
    half = partial.shape[3] // 2
    right = [(i, (i + 1) % count) for i in range(count)]
    left = [(i, (i - 1) % count) for i in range(count)]

    def block(step):
        return lax.dynamic_slice_in_dim(partial, ((me + step) % count) * rows, rows, axis=2)

    far = block(2)
    from_left = lax.ppermute(far[..., :half], axis, right)
    from_right = lax.ppermute(far[..., half:], axis, left)
    ahead, behind = block(1), block(count - 1)
    left_low = lax.ppermute(ahead[..., :half] + from_left, axis, right)
    left_high = lax.ppermute(ahead[..., half:], axis, right)
    right_low = lax.ppermute(behind[..., :half], axis, left)
    right_high = lax.ppermute(behind[..., half:] + from_right, axis, left)
    return block(0) + jnp.concatenate([left_low + right_low, left_high + right_high], axis=-1)


def shards(science, inv_variance, psf_kernel, offsets):
    radius = (psf_kernel.shape[0] - 1) // 2
    reach = MAXOFF * BR
    visits, rows, cols = science.shape
    total_rows = rows * lax.axis_size("sky")

    width = radius + reach
    count = lax.axis_size("sky")
    forward = [(i, i + 1) for i in range(count - 1)]
    backward = [(target, source) for source, target in forward]
    low = lax.ppermute(jnp.stack([science[:, rows - width :], inv_variance[:, rows - width :]]), "sky", forward)
    high = lax.ppermute(jnp.stack([science[:, :width], inv_variance[:, :width]]), "sky", backward)
    bordered = [
        jnp.concatenate([low[0] * low[1], science * inv_variance, high[0] * high[1]], axis=1),
        jnp.concatenate([low[1], inv_variance, high[1]], axis=1),
    ]

    psi = correlate_rows(bordered[0], toeplitz(psf_kernel, cols))
    phi = correlate_rows(bordered[1], toeplitz(psf_kernel * psf_kernel, cols))
    images = jnp.stack([psi, phi])

    first = lax.axis_index("sky") * rows - reach
    row_ids = first + lax.broadcasted_iota(jnp.int32, (1, 1, rows + 2 * reach, 1), 2)
    inside = (row_ids >= 0) & (row_ids < total_rows)
    images = jnp.where(inside, images, 0.0)

    mine = lax.dynamic_slice_in_dim(offsets, lax.axis_index("visit") * visits, visits, 0)
    shifts = range(-MAXOFF, MAXOFF + 1)
    onehot = jnp.stack([(mine == value).astype(jnp.float32) for value in shifts])
    windows = jnp.stack(
        [images[:, :, reach + value * BR : reach + value * BR + rows, :] for value in shifts], axis=1
    )
    partial = jnp.einsum(
        "otk,cotrw->ckrw", onehot, windows, precision=lax.Precision.HIGHEST
    )

    stacked = ring_reduce_scatter(partial, "visit")
    return stacked[0] / jnp.sqrt(stacked[1])


def solution(mesh):
    return jax.shard_map(
        shards,
        mesh=mesh,
        in_specs=(P("visit", "sky", None), P("visit", "sky", None), P(), P()),
        out_specs=P(None, ("sky", "visit"), None),
        check_vma=False,
    )
```

```python
import jax
import jax.numpy as jnp
from jax import lax
from jax.sharding import PartitionSpec as P

BR = 8
MAXOFF = 2


def bordered_rows(block, axis, width):
    count = lax.axis_size(axis)
    forward = [(i, i + 1) for i in range(count - 1)]
    backward = [(target, source) for source, target in forward]
    dim = block.ndim - 2
    low = lax.ppermute(
        lax.slice_in_dim(block, block.shape[dim] - width, None, axis=dim), axis, forward
    )
    high = lax.ppermute(lax.slice_in_dim(block, 0, width, axis=dim), axis, backward)
    return jnp.concatenate([low, block, high], axis=dim)


def toeplitz(taps, cols):
    size = taps.shape[1]
    radius = (size - 1) // 2
    w = lax.broadcasted_iota(jnp.int32, (1, cols, cols), 1)
    v = lax.broadcasted_iota(jnp.int32, (1, cols, cols), 2)
    tap = w - v + radius
    out = jnp.zeros((taps.shape[0], cols, cols), jnp.float32)
    for b in range(size):
        out = jnp.where(tap == b, taps[:, b][:, None, None], out)
    return out


def correlate_rows(bordered, kernel):
    n, extended, cols = bordered.shape
    out_rows = extended - kernel.shape[0] + 1
    joined = lax.conv_general_dilated(
        bordered.reshape(1, n * extended, cols),
        kernel,
        window_strides=(1,),
        padding=((0, kernel.shape[0] - 1),),
        dimension_numbers=("NHC", "HIO", "NHC"),
        precision=lax.Precision.HIGH,
        preferred_element_type=jnp.float32,
    )
    return joined.reshape(n, extended, cols)[:, :out_rows, :]


def ring_reduce_scatter(partial, axis):
    count = lax.axis_size(axis)
    if count != 4:
        return lax.psum_scatter(partial, axis, scatter_dimension=2, tiled=True)
    me = lax.axis_index(axis)
    rows = partial.shape[2] // count
    half = partial.shape[3] // 2
    right = [(i, (i + 1) % count) for i in range(count)]
    left = [(i, (i - 1) % count) for i in range(count)]

    def block(step):
        return lax.dynamic_slice_in_dim(partial, ((me + step) % count) * rows, rows, axis=2)

    far = block(2)
    from_left = lax.ppermute(far[..., :half], axis, right)
    from_right = lax.ppermute(far[..., half:], axis, left)
    ahead = block(1)
    ahead = jnp.concatenate([ahead[..., :half] + from_left, ahead[..., half:]], axis=-1)
    behind = block(count - 1)
    behind = jnp.concatenate([behind[..., :half], behind[..., half:] + from_right], axis=-1)
    got_left = lax.ppermute(ahead, axis, right)
    got_right = lax.ppermute(behind, axis, left)
    return block(0) + got_left + got_right


def shards(science, inv_variance, psf_kernel, offsets):
    radius = (psf_kernel.shape[0] - 1) // 2
    reach = MAXOFF * BR
    visits, rows, cols = science.shape
    total_rows = rows * lax.axis_size("sky")

    width = radius + reach
    count = lax.axis_size("sky")
    forward = [(i, i + 1) for i in range(count - 1)]
    backward = [(target, source) for source, target in forward]
    low = lax.ppermute(jnp.stack([science[:, rows - width :], inv_variance[:, rows - width :]]), "sky", forward)
    high = lax.ppermute(jnp.stack([science[:, :width], inv_variance[:, :width]]), "sky", backward)
    bordered = [
        jnp.concatenate([low[0] * low[1], science * inv_variance, high[0] * high[1]], axis=1),
        jnp.concatenate([low[1], inv_variance, high[1]], axis=1),
    ]

    psi = correlate_rows(bordered[0], toeplitz(psf_kernel, cols))
    phi = correlate_rows(bordered[1], toeplitz(psf_kernel * psf_kernel, cols))
    images = jnp.stack([psi, phi])

    first = lax.axis_index("sky") * rows - reach
    row_ids = first + lax.broadcasted_iota(jnp.int32, (1, 1, rows + 2 * reach, 1), 2)
    inside = (row_ids >= 0) & (row_ids < total_rows)
    images = jnp.where(inside, images, 0.0)

    mine = lax.dynamic_slice_in_dim(offsets, lax.axis_index("visit") * visits, visits, 0)
    shifts = range(-MAXOFF, MAXOFF + 1)
    onehot = jnp.stack([(mine == value).astype(jnp.float32) for value in shifts])
    windows = jnp.stack(
        [images[:, :, reach + value * BR : reach + value * BR + rows, :] for value in shifts], axis=1
    )
    partial = jnp.einsum(
        "otk,cotrw->ckrw", onehot, windows, precision=lax.Precision.HIGHEST
    )

    stacked = ring_reduce_scatter(partial, "visit")
    return stacked[0] / jnp.sqrt(stacked[1])


def solution(mesh):
    return jax.shard_map(
        shards,
        mesh=mesh,
        in_specs=(P("visit", "sky", None), P("visit", "sky", None), P(), P()),
        out_specs=P(None, ("sky", "visit"), None),
        check_vma=False,
    )
```

```python
import jax
import jax.numpy as jnp
from jax import lax
from jax.sharding import PartitionSpec as P

BR = 8
MAXOFF = 2


def bordered_rows(block, axis, width):
    count = lax.axis_size(axis)
    forward = [(i, i + 1) for i in range(count - 1)]
    backward = [(target, source) for source, target in forward]
    dim = block.ndim - 2
    low = lax.ppermute(
        lax.slice_in_dim(block, block.shape[dim] - width, None, axis=dim), axis, forward
    )
    high = lax.ppermute(lax.slice_in_dim(block, 0, width, axis=dim), axis, backward)
    return jnp.concatenate([low, block, high], axis=dim)


def toeplitz(taps, cols):
    size = taps.shape[1]
    radius = (size - 1) // 2
    w = lax.broadcasted_iota(jnp.int32, (1, cols, cols), 1)
    v = lax.broadcasted_iota(jnp.int32, (1, cols, cols), 2)
    tap = w - v + radius
    out = jnp.zeros((taps.shape[0], cols, cols), jnp.float32)
    for b in range(size):
        out = jnp.where(tap == b, taps[:, b][:, None, None], out)
    return out


def correlate_rows(bordered, kernel):
    return lax.conv_general_dilated(
        bordered,
        kernel,
        window_strides=(1,),
        padding="VALID",
        dimension_numbers=("NHC", "HIO", "NHC"),
        precision=lax.Precision.HIGH,
        preferred_element_type=jnp.float32,
    )


def ring_reduce_scatter(partial, axis):
    count = lax.axis_size(axis)
    if count != 4:
        return lax.psum_scatter(partial, axis, scatter_dimension=2, tiled=True)
    me = lax.axis_index(axis)
    rows = partial.shape[2] // count
    half = partial.shape[3] // 2
    right = [(i, (i + 1) % count) for i in range(count)]
    left = [(i, (i - 1) % count) for i in range(count)]

    def block(step):
        return lax.dynamic_slice_in_dim(partial, ((me + step) % count) * rows, rows, axis=2)

    far = block(2)
    from_left = lax.ppermute(far[..., :half], axis, right)
    from_right = lax.ppermute(far[..., half:], axis, left)
    ahead = block(1)
    ahead = jnp.concatenate([ahead[..., :half] + from_left, ahead[..., half:]], axis=-1)
    behind = block(count - 1)
    behind = jnp.concatenate([behind[..., :half], behind[..., half:] + from_right], axis=-1)
    got_left = lax.ppermute(ahead, axis, right)
    got_right = lax.ppermute(behind, axis, left)
    return block(0) + got_left + got_right


def shards(science, inv_variance, psf_kernel, offsets):
    radius = (psf_kernel.shape[0] - 1) // 2
    reach = MAXOFF * BR
    visits, rows, cols = science.shape
    total_rows = rows * lax.axis_size("sky")

    width = radius + reach
    count = lax.axis_size("sky")
    forward = [(i, i + 1) for i in range(count - 1)]
    backward = [(target, source) for source, target in forward]
    low = lax.ppermute(jnp.stack([science[:, rows - width :], inv_variance[:, rows - width :]]), "sky", forward)
    high = lax.ppermute(jnp.stack([science[:, :width], inv_variance[:, :width]]), "sky", backward)
    bordered = [
        jnp.concatenate([low[0] * low[1], science * inv_variance, high[0] * high[1]], axis=1),
        jnp.concatenate([low[1], inv_variance, high[1]], axis=1),
    ]

    psi = correlate_rows(bordered[0], toeplitz(psf_kernel, cols))
    phi = correlate_rows(bordered[1], toeplitz(psf_kernel * psf_kernel, cols))
    images = jnp.stack([psi, phi])

    first = lax.axis_index("sky") * rows - reach
    row_ids = first + lax.broadcasted_iota(jnp.int32, (1, 1, rows + 2 * reach, 1), 2)
    inside = (row_ids >= 0) & (row_ids < total_rows)
    images = jnp.where(inside, images, 0.0)

    mine = lax.dynamic_slice_in_dim(offsets, lax.axis_index("visit") * visits, visits, 0)
    shifts = range(-MAXOFF, MAXOFF + 1)
    onehot = jnp.stack([(mine == value).astype(jnp.float32) for value in shifts])
    windows = jnp.stack(
        [images[:, :, reach + value * BR : reach + value * BR + rows, :] for value in shifts], axis=1
    )
    partial = jnp.einsum(
        "otk,cotrw->ckrw", onehot, windows, precision=lax.Precision.HIGH
    )

    stacked = ring_reduce_scatter(partial, "visit")
    return stacked[0] / jnp.sqrt(stacked[1])


def solution(mesh):
    return jax.shard_map(
        shards,
        mesh=mesh,
        in_specs=(P("visit", "sky", None), P("visit", "sky", None), P(), P()),
        out_specs=P(None, ("sky", "visit"), None),
        check_vma=False,
    )
```

```python
import jax
import jax.numpy as jnp
from jax import lax
from jax.sharding import PartitionSpec as P

BR = 8
MAXOFF = 2


def bordered_rows(block, axis, width):
    count = lax.axis_size(axis)
    forward = [(i, i + 1) for i in range(count - 1)]
    backward = [(target, source) for source, target in forward]
    dim = block.ndim - 2
    low = lax.ppermute(
        lax.slice_in_dim(block, block.shape[dim] - width, None, axis=dim), axis, forward
    )
    high = lax.ppermute(lax.slice_in_dim(block, 0, width, axis=dim), axis, backward)
    return jnp.concatenate([low, block, high], axis=dim)


def toeplitz(taps, cols):
    size = taps.shape[1]
    radius = (size - 1) // 2
    w = lax.broadcasted_iota(jnp.int32, (1, cols, cols), 1)
    v = lax.broadcasted_iota(jnp.int32, (1, cols, cols), 2)
    tap = w - v + radius
    out = jnp.zeros((taps.shape[0], cols, cols), jnp.float32)
    for b in range(size):
        out = jnp.where(tap == b, taps[:, b][:, None, None], out)
    return out


def correlate_rows(bordered, kernel):
    return lax.conv_general_dilated(
        bordered,
        kernel,
        window_strides=(1,),
        padding="VALID",
        dimension_numbers=("NHC", "HIO", "NHC"),
        precision=lax.Precision.HIGH,
        preferred_element_type=jnp.float32,
    )


def ring_reduce_scatter(partial, axis):
    count = lax.axis_size(axis)
    if count != 4:
        return lax.psum_scatter(partial, axis, scatter_dimension=2, tiled=True)
    me = lax.axis_index(axis)
    rows = partial.shape[2] // count
    half = partial.shape[1] // 2
    right = [(i, (i + 1) % count) for i in range(count)]
    left = [(i, (i - 1) % count) for i in range(count)]

    def block(step):
        return lax.dynamic_slice_in_dim(partial, ((me + step) % count) * rows, rows, axis=2)

    far = block(2)
    from_left = lax.ppermute(far[:, :half], axis, right)
    from_right = lax.ppermute(far[:, half:], axis, left)
    ahead = block(1)
    ahead = jnp.concatenate([ahead[:, :half] + from_left, ahead[:, half:]], axis=1)
    behind = block(count - 1)
    behind = jnp.concatenate([behind[:, :half], behind[:, half:] + from_right], axis=1)
    got_left = lax.ppermute(ahead, axis, right)
    got_right = lax.ppermute(behind, axis, left)
    return block(0) + got_left + got_right


def shards(science, inv_variance, psf_kernel, offsets):
    radius = (psf_kernel.shape[0] - 1) // 2
    reach = MAXOFF * BR
    visits, rows, cols = science.shape
    total_rows = rows * lax.axis_size("sky")

    width = radius + reach
    count = lax.axis_size("sky")
    forward = [(i, i + 1) for i in range(count - 1)]
    backward = [(target, source) for source, target in forward]
    low = lax.ppermute(jnp.stack([science[:, rows - width :], inv_variance[:, rows - width :]]), "sky", forward)
    high = lax.ppermute(jnp.stack([science[:, :width], inv_variance[:, :width]]), "sky", backward)
    bordered = [
        jnp.concatenate([low[0] * low[1], science * inv_variance, high[0] * high[1]], axis=1),
        jnp.concatenate([low[1], inv_variance, high[1]], axis=1),
    ]

    psi = correlate_rows(bordered[0], toeplitz(psf_kernel, cols))
    phi = correlate_rows(bordered[1], toeplitz(psf_kernel * psf_kernel, cols))
    images = jnp.stack([psi, phi])

    first = lax.axis_index("sky") * rows - reach
    row_ids = first + lax.broadcasted_iota(jnp.int32, (1, 1, rows + 2 * reach, 1), 2)
    inside = (row_ids >= 0) & (row_ids < total_rows)
    images = jnp.where(inside, images, 0.0)

    mine = lax.dynamic_slice_in_dim(offsets, lax.axis_index("visit") * visits, visits, 0)
    shifts = range(-MAXOFF, MAXOFF + 1)
    onehot = jnp.stack([(mine == value).astype(jnp.float32) for value in shifts])
    windows = jnp.stack(
        [images[:, :, reach + value * BR : reach + value * BR + rows, :] for value in shifts], axis=1
    )
    partial = jnp.einsum(
        "otk,cotrw->ckrw", onehot, windows, precision=lax.Precision.HIGH
    )

    stacked = ring_reduce_scatter(partial, "visit")
    return stacked[0] / jnp.sqrt(stacked[1])


def solution(mesh):
    return jax.shard_map(
        shards,
        mesh=mesh,
        in_specs=(P("visit", "sky", None), P("visit", "sky", None), P(), P()),
        out_specs=P(None, ("sky", "visit"), None),
        check_vma=False,
    )
```

```python
import jax
import jax.numpy as jnp
from jax import lax
from jax.sharding import PartitionSpec as P

BR = 8
MAXOFF = 2


def bordered_rows(block, axis, width):
    count = lax.axis_size(axis)
    forward = [(i, i + 1) for i in range(count - 1)]
    backward = [(target, source) for source, target in forward]
    dim = block.ndim - 2
    low = lax.ppermute(
        lax.slice_in_dim(block, block.shape[dim] - width, None, axis=dim), axis, forward
    )
    high = lax.ppermute(lax.slice_in_dim(block, 0, width, axis=dim), axis, backward)
    return jnp.concatenate([low, block, high], axis=dim)


def toeplitz(taps, cols):
    size = taps.shape[1]
    radius = (size - 1) // 2
    w = lax.broadcasted_iota(jnp.int32, (1, cols, cols), 1)
    v = lax.broadcasted_iota(jnp.int32, (1, cols, cols), 2)
    tap = w - v + radius
    out = jnp.zeros((taps.shape[0], cols, cols), jnp.float32)
    for b in range(size):
        out = jnp.where(tap == b, taps[:, b][:, None, None], out)
    return out


def correlate_rows(bordered, kernel):
    return lax.conv_general_dilated(
        bordered,
        kernel,
        window_strides=(1,),
        padding="VALID",
        dimension_numbers=("NHC", "HIO", "NHC"),
        precision=lax.Precision.HIGH,
        preferred_element_type=jnp.float32,
    )


def ring_reduce_scatter(partial, axis):
    count = lax.axis_size(axis)
    if count != 4:
        return lax.psum_scatter(partial, axis, scatter_dimension=2, tiled=True)
    me = lax.axis_index(axis)
    rows = partial.shape[2] // count
    half = partial.shape[1] // 2
    right = [(i, (i + 1) % count) for i in range(count)]
    left = [(i, (i - 1) % count) for i in range(count)]

    def block(step):
        return lax.dynamic_slice_in_dim(partial, ((me + step) % count) * rows, rows, axis=2)

    far = block(2)
    from_left = lax.ppermute(far[:, :half], axis, right)
    from_right = lax.ppermute(far[:, half:], axis, left)
    ahead, behind, from_left, from_right = lax.optimization_barrier(
        (block(1), block(count - 1), from_left, from_right)
    )
    ahead = lax.dynamic_update_slice_in_dim(ahead, ahead[:, :half] + from_left, 0, axis=1)
    behind = lax.dynamic_update_slice_in_dim(behind, behind[:, half:] + from_right, half, axis=1)
    got_left = lax.ppermute(ahead, axis, right)
    got_right = lax.ppermute(behind, axis, left)
    return block(0) + got_left + got_right


def shards(science, inv_variance, psf_kernel, offsets):
    radius = (psf_kernel.shape[0] - 1) // 2
    reach = MAXOFF * BR
    visits, rows, cols = science.shape
    total_rows = rows * lax.axis_size("sky")

    width = radius + reach
    count = lax.axis_size("sky")
    forward = [(i, i + 1) for i in range(count - 1)]
    backward = [(target, source) for source, target in forward]
    low = lax.ppermute(jnp.stack([science[:, rows - width :], inv_variance[:, rows - width :]]), "sky", forward)
    high = lax.ppermute(jnp.stack([science[:, :width], inv_variance[:, :width]]), "sky", backward)
    bordered = [
        jnp.concatenate([low[0] * low[1], science * inv_variance, high[0] * high[1]], axis=1),
        jnp.concatenate([low[1], inv_variance, high[1]], axis=1),
    ]

    psi = correlate_rows(bordered[0], toeplitz(psf_kernel, cols))
    phi = correlate_rows(bordered[1], toeplitz(psf_kernel * psf_kernel, cols))
    images = jnp.stack([psi, phi])

    first = lax.axis_index("sky") * rows - reach
    row_ids = first + lax.broadcasted_iota(jnp.int32, (1, 1, rows + 2 * reach, 1), 2)
    inside = (row_ids >= 0) & (row_ids < total_rows)
    images = jnp.where(inside, images, 0.0)

    mine = lax.dynamic_slice_in_dim(offsets, lax.axis_index("visit") * visits, visits, 0)
    shifts = range(-MAXOFF, MAXOFF + 1)
    onehot = jnp.stack([(mine == value).astype(jnp.float32) for value in shifts])
    windows = jnp.stack(
        [images[:, :, reach + value * BR : reach + value * BR + rows, :] for value in shifts], axis=1
    )
    partial = jnp.einsum(
        "otk,cotrw->ckrw", onehot, windows, precision=lax.Precision.HIGH
    )

    stacked = ring_reduce_scatter(partial, "visit")
    return stacked[0] / jnp.sqrt(stacked[1])


def solution(mesh):
    return jax.shard_map(
        shards,
        mesh=mesh,
        in_specs=(P("visit", "sky", None), P("visit", "sky", None), P(), P()),
        out_specs=P(None, ("sky", "visit"), None),
        check_vma=False,
    )
```

```python
import jax
import jax.numpy as jnp
from jax import lax
from jax.sharding import PartitionSpec as P

BR = 8
MAXOFF = 2


def bordered_rows(block, axis, width):
    count = lax.axis_size(axis)
    forward = [(i, i + 1) for i in range(count - 1)]
    backward = [(target, source) for source, target in forward]
    dim = block.ndim - 2
    low = lax.ppermute(
        lax.slice_in_dim(block, block.shape[dim] - width, None, axis=dim), axis, forward
    )
    high = lax.ppermute(lax.slice_in_dim(block, 0, width, axis=dim), axis, backward)
    return jnp.concatenate([low, block, high], axis=dim)


def toeplitz(taps, cols):
    size = taps.shape[1]
    radius = (size - 1) // 2
    w = lax.broadcasted_iota(jnp.int32, (1, cols, cols), 1)
    v = lax.broadcasted_iota(jnp.int32, (1, cols, cols), 2)
    tap = w - v + radius
    out = jnp.zeros((taps.shape[0], cols, cols), jnp.float32)
    for b in range(size):
        out = jnp.where(tap == b, taps[:, b][:, None, None], out)
    return out


def correlate_rows(bordered, kernel):
    return lax.conv_general_dilated(
        bordered,
        kernel,
        window_strides=(1,),
        padding="VALID",
        dimension_numbers=("NHC", "HIO", "NHC"),
        precision=lax.Precision.HIGH,
        preferred_element_type=jnp.float32,
    )


def ring_reduce_scatter(partial, axis):
    count = lax.axis_size(axis)
    if count != 4:
        return lax.psum_scatter(partial, axis, scatter_dimension=2, tiled=True)
    me = lax.axis_index(axis)
    rows = partial.shape[2] // count
    half = partial.shape[1] // 2
    right = [(i, (i + 1) % count) for i in range(count)]
    left = [(i, (i - 1) % count) for i in range(count)]

    def block(step):
        return lax.dynamic_slice_in_dim(partial, ((me + step) % count) * rows, rows, axis=2)

    far = block(2)
    from_left = lax.ppermute(far[:, :half], axis, right)
    from_right = lax.ppermute(far[:, half:], axis, left)
    ahead = block(1)
    ahead = jnp.concatenate([ahead[:, :half] + from_left, ahead[:, half:]], axis=1)
    behind = block(count - 1)
    behind = jnp.concatenate([behind[:, :half], behind[:, half:] + from_right], axis=1)
    got_left = lax.ppermute(ahead, axis, right)
    got_right = lax.ppermute(behind, axis, left)
    return block(0) + got_left + got_right


def shards(science, inv_variance, psf_kernel, offsets):
    radius = (psf_kernel.shape[0] - 1) // 2
    reach = MAXOFF * BR
    visits, rows, cols = science.shape
    total_rows = rows * lax.axis_size("sky")

    width = radius + reach
    count = lax.axis_size("sky")
    forward = [(i, i + 1) for i in range(count - 1)]
    backward = [(target, source) for source, target in forward]
    low = lax.ppermute(jnp.stack([science[:, rows - width :], inv_variance[:, rows - width :]]), "sky", forward)
    high = lax.ppermute(jnp.stack([science[:, :width], inv_variance[:, :width]]), "sky", backward)
    bordered = jnp.concatenate(
        [
            jnp.concatenate([low[0] * low[1], science * inv_variance, high[0] * high[1]], axis=1),
            jnp.concatenate([low[1], inv_variance, high[1]], axis=1),
        ],
        axis=2,
    )

    kernel = jnp.concatenate([toeplitz(psf_kernel, cols), toeplitz(psf_kernel * psf_kernel, cols)], axis=2)
    both = lax.conv_general_dilated(
        bordered,
        kernel,
        window_strides=(1,),
        padding="VALID",
        dimension_numbers=("NHC", "HIO", "NHC"),
        feature_group_count=2,
        precision=lax.Precision.HIGH,
        preferred_element_type=jnp.float32,
    )
    images = jnp.stack([both[..., :cols], both[..., cols:]])

    first = lax.axis_index("sky") * rows - reach
    row_ids = first + lax.broadcasted_iota(jnp.int32, (1, 1, rows + 2 * reach, 1), 2)
    inside = (row_ids >= 0) & (row_ids < total_rows)
    images = jnp.where(inside, images, 0.0)

    mine = lax.dynamic_slice_in_dim(offsets, lax.axis_index("visit") * visits, visits, 0)
    shifts = range(-MAXOFF, MAXOFF + 1)
    onehot = jnp.stack([(mine == value).astype(jnp.float32) for value in shifts])
    windows = jnp.stack(
        [images[:, :, reach + value * BR : reach + value * BR + rows, :] for value in shifts], axis=1
    )
    partial = jnp.einsum(
        "otk,cotrw->ckrw", onehot, windows, precision=lax.Precision.HIGH
    )

    stacked = ring_reduce_scatter(partial, "visit")
    return stacked[0] / jnp.sqrt(stacked[1])


def solution(mesh):
    return jax.shard_map(
        shards,
        mesh=mesh,
        in_specs=(P("visit", "sky", None), P("visit", "sky", None), P(), P()),
        out_specs=P(None, ("sky", "visit"), None),
        check_vma=False,
    )
```
